256 devices in a mesh: ctx: 8 (over x, core), ch: 32 (over y, z).
Axes of the slice: x: 4, y: 4, z: 8, core: 2. Of those that a mesh axis runs over, the one named last changes fastest.
Arguments:
- tokens_in: bfloat16 [8192, 8192], P(('ctx', 'ch')), may hold values from -6 to 6
- norm_gain: float32 [8192], replicated, may hold values from 0.1 to 1.9
- proj_weight: bfloat16 [3, 8192, 8192], P(None, 'ctx', 'ch'), may hold values from -0.0625 to 0.0625
- conv_weight: float32 [3, 7, 8192], P(None, None, 'ch'), may hold values from -2 to 2
- decay_rate: float32 [16, 8192], P(None, 'ch'), may hold values from 6.1035157e-06 to 0.04
- residue: float32 [16, 8192], P(None, 'ch'), may hold values from -1.5 to 1.5
- skip_gain: float32 [8192], P('ch'), may hold values from -3 to 3
Outputs:
- gated: bfloat16 [8192, 8192], P(('ctx', 'ch'))
The draws below stay inside these ranges and needn't reach their ends.
All inputs are finite; a program needn't handle non-finite values.
Results may differ from the reference program's by a relative error of at most 0.008.
Values may be sent and summed in bfloat16 or wider, within the bound.
No kernel may reach another device: no remote copies, remote signals or barrier semaphores. Data moves between devices by JAX's collectives and lax.ppermute only.
A program may use at most 128 MiB of HBM per device.

```python
import math
import jax
import jax.numpy as jnp
from jax import lax

D = 8192
MODES = 16
TAPS = 7
TOKENS = 8192


def levels(rng, dims, pieces, least, top_value):
    def one(axis_at, shards_of):
        draws = jax.random.uniform(jax.random.fold_in(jax.random.fold_in(rng, 6), axis_at), (shards_of,), jnp.float32, least / len(pieces), top_value / len(pieces))
        return jnp.repeat(jnp.exp(draws), dims[axis_at] // shards_of).reshape((-1,) + (1,) * (len(dims) - axis_at - 1))

    loudness = one(*pieces[0])
    for cut in pieces[1:]:
        loudness = loudness * one(*cut)
    return loudness


def centred(stream_key, dims, spread, limit, pieces=(), dtype=jnp.bfloat16):
    drawn = spread * jax.random.normal(stream_key, dims, jnp.float32)
    if pieces:
        drawn = drawn * levels(stream_key, dims, pieces, -0.22, 0.18)
    return jnp.clip(drawn, -limit, limit).astype(dtype)


def setup_inputs(seed: int = 0) -> dict:
    splits = jax.random.split(jax.random.key(seed), 8)
    return {
        "tokens_in": centred(splits[0], (TOKENS, D), 1.0, 6.0, ((0, 256),)),
        "norm_gain": jnp.clip(1.0 + 0.18 * jax.random.normal(splits[1], (D,), jnp.float32), 0.1, 1.9),
        "proj_weight": centred(splits[2], (3, D, D), D ** -0.5, 0.0625, ((1, 8), (2, 32))),
        "conv_weight": centred(splits[3], (3, TAPS, D), 0.4, 2.0, ((2, 32),), jnp.float32),
        "decay_rate": jnp.clip(jnp.exp(math.log(0.04) - 8.78776976 * jax.random.uniform(splits[4], (MODES, D), jnp.float32) ** levels(splits[4], (MODES, D), ((1, 32),), -0.2, 0.2)), 6.10351571594947e-06, 0.04),
        "residue": centred(splits[5], (MODES, D), 0.25, 1.5, ((1, 32),), jnp.float32),
        "skip_gain": centred(splits[6], (D,), 0.5, 3.0, ((0, 32),), jnp.float32),
    }


norm_eps = 1e-05

def reference(tokens_in, norm_gain, proj_weight, conv_weight, decay_rate, residue, skip_gain):
    widened = tokens_in.astype(jnp.float32)
    mean_square = lax.optimization_barrier(jnp.mean(widened * widened, axis=-1, keepdims=True))
    normed = (widened * lax.rsqrt(mean_square + norm_eps) * norm_gain[None, :]).astype(jnp.bfloat16)
    normed_wide = normed.astype(jnp.float32)

    def project_one(weight_one):
        product = jnp.dot(normed_wide, weight_one.astype(jnp.float32), precision=lax.Precision.HIGHEST)
        return product.astype(jnp.bfloat16)
    projected = lax.map(project_one, proj_weight)
    row_count = projected.shape[1]
    reach = TAPS - 1
    padded = jnp.pad(projected.astype(jnp.float32), ((0, 0), (reach, 0), (0, 0)))
    featured = jnp.zeros(projected.shape, jnp.float32)
    for shift_idx in range(TAPS):
        featured = featured + conv_weight[:, shift_idx, None, :] * padded[:, reach - shift_idx:reach - shift_idx + row_count, :]
    mixed = featured[1] * featured[2]
    retention = jnp.exp(-decay_rate)
    in_scale = jnp.sqrt(-jnp.expm1(-2.0 * decay_rate))

    def advance(carried, mixed_row):
        carried = retention * carried + in_scale * mixed_row[None, :]
        return (carried, lax.optimization_barrier(jnp.sum(residue * carried, axis=0)))
    start_state = jnp.zeros(decay_rate.shape, jnp.float32)
    final_state, filtered = lax.scan(advance, start_state, mixed)
    gated = featured[0] * (filtered + skip_gain[None, :] * mixed)
    return gated.astype(jnp.bfloat16)
```

```python
import jax
import jax.numpy as jnp
from jax import lax
from jax.sharding import PartitionSpec as P

norm_eps = 1e-05


def shifted(shard, axis, by):
    length = lax.axis_size(axis)
    pairs = [(i, i + by) for i in range(length) if 0 <= i + by < length]
    return lax.ppermute(shard, axis, pairs)


def gathered_weight(block):
    count = lax.axis_size("ctx")
    me = lax.axis_index("ctx")
    width = block.shape[1]
    held = [(block, me)]
    for by in range(2, count, 2):
        pairs = [(i, (i + by) % count) for i in range(count)]
        held.append((lax.ppermute(block, "ctx", pairs), (me - by) % count))
    sibling = [(i, i ^ 1) for i in range(count)]
    forwarded = [(lax.ppermute(part, "ctx", sibling), src ^ 1) for part, src in held]
    full = jnp.zeros((block.shape[0], count * width, block.shape[2]), block.dtype)
    for part, src in held + forwarded:
        full = lax.dynamic_update_slice(full, part, (0, src * width, 0))
    return full


def on_device(tokens_in, norm_gain, proj_weight, conv_weight, decay_rate, residue, skip_gain):
    widened = tokens_in.astype(jnp.float32)
    mean_square = jnp.mean(widened * widened, axis=-1, keepdims=True)
    normed = (widened * lax.rsqrt(mean_square + norm_eps) * norm_gain[None, :]).astype(jnp.bfloat16)
    gathered = lax.all_gather(normed, "ch", axis=0, tiled=True)
    row_count = gathered.shape[0]
    chan_count = proj_weight.shape[2]
    summed = jnp.einsum(
        "tf,ifc->itc",
        gathered,
        gathered_weight(proj_weight),
        preferred_element_type=jnp.float32,
    )
    projected = summed.astype(jnp.bfloat16)
    tap_count = conv_weight.shape[1]
    reach = tap_count - 1
    rim_rows = shifted(projected[:, row_count - reach :, :], "ctx", 1)
    padded = jnp.concatenate([rim_rows, projected], axis=1).astype(jnp.float32)
    featured = jnp.zeros((3, row_count, chan_count), jnp.float32)
    for shift_idx in range(tap_count):
        featured = (
            featured
            + conv_weight[:, shift_idx, None, :]
            * padded[:, reach - shift_idx : reach - shift_idx + row_count, :]
        )
    queries = featured[0]
    mixed = featured[1] * featured[2]
    highest = lax.Precision.HIGHEST
    in_scale = jnp.sqrt(-jnp.expm1(-2.0 * decay_rate))
    span_rows = min(128, row_count)
    span_count = row_count // span_rows
    positions = jnp.arange(span_rows, dtype=jnp.float32)
    lag_decay = jnp.exp(-decay_rate[:, None, :] * positions[None, :, None])
    impulse = jnp.sum((residue * in_scale)[:, None, :] * lag_decay, axis=0)
    offsets = jnp.arange(span_rows)[:, None] - jnp.arange(span_rows)[None, :]
    lag_table = (offsets[None, :, :] == jnp.arange(span_rows)[:, None, None]).astype(jnp.float32)
    toeplitz = jnp.einsum("lc,lts->cts", impulse, lag_table, precision=highest)
    spans_in = mixed.reshape(span_count, span_rows, chan_count)
    inside = jnp.einsum("cts,jsc->jtc", toeplitz, spans_in, precision=highest)
    end_weight = in_scale[:, None, :] * jnp.exp(
        -decay_rate[:, None, :] * (span_rows - 1.0 - positions)[None, :, None]
    )
    span_ends = jnp.einsum("jsc,msc->jmc", spans_in, end_weight, precision=highest)
    span_decay = jnp.exp(-decay_rate * float(span_rows))

    def advance(carried, span_end):
        return (span_decay * carried + span_end, carried)

    zero_state = jnp.zeros(decay_rate.shape, jnp.float32)
    local_end, starts = lax.scan(advance, zero_state, span_ends)
    range_count = lax.axis_size("ctx")
    range_idx = lax.axis_index("ctx")
    all_ends = lax.all_gather(local_end, "ctx", axis=0)
    earlier = jnp.arange(range_count)
    lag = jnp.maximum(range_idx - 1 - earlier, 0).astype(jnp.float32)
    lag_decay_ends = jnp.where(
        (earlier < range_idx)[:, None, None],
        jnp.exp(-decay_rate[None, :, :] * (float(row_count) * lag)[:, None, None]),
        0.0,
    )
    incoming = jnp.sum(lag_decay_ends * all_ends, axis=0)
    span_starts = jnp.arange(span_count, dtype=jnp.float32) * float(span_rows)
    starts = (
        starts
        + jnp.exp(-decay_rate[None, :, :] * span_starts[:, None, None]) * incoming[None, :, :]
    )
    out_weight = residue[:, None, :] * jnp.exp(
        -decay_rate[:, None, :] * (positions + 1.0)[None, :, None]
    )
    outside = jnp.einsum("jmc,mtc->jtc", starts, out_weight, precision=highest)
    filtered = (inside + outside).reshape(row_count, chan_count)
    gated = (queries * (filtered + skip_gain[None, :] * mixed)).astype(jnp.bfloat16)
    return lax.all_to_all(gated, "ch", split_axis=0, concat_axis=1, tiled=True)


def solution(mesh):
    in_specs = (
        P(("ctx", "ch"), None),
        P(),
        P(None, "ctx", "ch"),
        P(None, None, "ch"),
        P(None, "ch"),
        P(None, "ch"),
        P("ch"),
    )
    out_specs = P(("ctx", "ch"), None)
    return jax.shard_map(
        on_device, mesh=mesh, in_specs=in_specs, out_specs=out_specs, check_vma=False
    )
```

```python
import jax
import jax.numpy as jnp
from jax import lax
from jax.sharding import PartitionSpec as P

norm_eps = 1e-05


def shifted(shard, axis, by):
    length = lax.axis_size(axis)
    pairs = [(i, i + by) for i in range(length) if 0 <= i + by < length]
    return lax.ppermute(shard, axis, pairs)


def gathered_weight(block):
    count = lax.axis_size("ctx")
    me = lax.axis_index("ctx")
    width = block.shape[1]
    held = [(block, me)]
    for by in range(2, count, 2):
        pairs = [(i, (i + by) % count) for i in range(count)]
        held.append((lax.ppermute(block, "ctx", pairs), (me - by) % count))
    sibling = [(i, i ^ 1) for i in range(count)]
    forwarded = [(lax.ppermute(part, "ctx", sibling), src ^ 1) for part, src in held]
    full = jnp.zeros((block.shape[0], count * width, block.shape[2]), block.dtype)
    for part, src in held + forwarded:
        full = lax.dynamic_update_slice(full, part, (0, src * width, 0))
    return full


def on_device_body(tokens_in, norm_gain, proj_weight, conv_weight, decay_rate, residue, skip_gain):
    widened = tokens_in.astype(jnp.float32)
    mean_square = jnp.mean(widened * widened, axis=-1, keepdims=True)
    normed = (widened * lax.rsqrt(mean_square + norm_eps) * norm_gain[None, :]).astype(jnp.bfloat16)
    gathered = lax.all_gather(normed, "ch", axis=0, tiled=True)
    row_count = gathered.shape[0]
    chan_count = proj_weight.shape[2]
    summed = jnp.einsum(
        "tf,ifc->itc",
        gathered,
        gathered_weight(proj_weight),
        preferred_element_type=jnp.float32,
    )
    projected = summed.astype(jnp.bfloat16)
    tap_count = conv_weight.shape[1]
    reach = tap_count - 1
    rim_rows = shifted(projected[:, row_count - reach :, :], "ctx", 1)
    padded = jnp.concatenate([rim_rows, projected], axis=1).astype(jnp.float32)
    featured = jnp.zeros((3, row_count, chan_count), jnp.float32)
    for shift_idx in range(tap_count):
        featured = (
            featured
            + conv_weight[:, shift_idx, None, :]
            * padded[:, reach - shift_idx : reach - shift_idx + row_count, :]
        )
    queries = featured[0]
    mixed = featured[1] * featured[2]
    highest = lax.Precision.HIGHEST
    high = lax.Precision.HIGH
    in_scale = jnp.sqrt(-jnp.expm1(-2.0 * decay_rate))
    span_rows = min(128, row_count)
    span_count = row_count // span_rows
    positions = jnp.arange(span_rows, dtype=jnp.float32)
    own_rate, own_residue = lax.optimization_barrier((decay_rate, residue))
    own_scale = jnp.sqrt(-jnp.expm1(-2.0 * own_rate))
    lag_decay = jnp.exp(-own_rate[:, None, :] * positions[None, :, None])
    impulse = jnp.sum((own_residue * own_scale)[:, None, :] * lag_decay, axis=0)
    offsets = jnp.arange(span_rows)[:, None] - jnp.arange(span_rows)[None, :]
    lag_table = (offsets[None, :, :] == jnp.arange(span_rows)[:, None, None]).astype(jnp.float32)
    toeplitz = jnp.einsum("lc,lts->cts", impulse, lag_table, precision=highest)
    toeplitz = lax.optimization_barrier(toeplitz)
    spans_in = mixed.reshape(span_count, span_rows, chan_count)
    inside = jnp.einsum("cts,jsc->jtc", toeplitz, spans_in, precision=high)
    end_weight = in_scale[:, None, :] * jnp.exp(
        -decay_rate[:, None, :] * (span_rows - 1.0 - positions)[None, :, None]
    )
    span_ends = jnp.einsum("jsc,msc->jmc", spans_in, end_weight, precision=high)
    span_decay = jnp.exp(-decay_rate * float(span_rows))

    def advance(carried, span_end):
        return (span_decay * carried + span_end, carried)

    zero_state = jnp.zeros(decay_rate.shape, jnp.float32)
    local_end, starts = lax.scan(advance, zero_state, span_ends)
    incoming = zero_state
    for by in range(1, lax.axis_size("ctx")):
        carried_end = shifted(local_end, "ctx", by)
        incoming = incoming + jnp.exp(-decay_rate * float(row_count * (by - 1))) * carried_end
    span_starts = jnp.arange(span_count, dtype=jnp.float32) * float(span_rows)
    starts = (
        starts
        + jnp.exp(-decay_rate[None, :, :] * span_starts[:, None, None]) * incoming[None, :, :]
    )
    out_weight = residue[:, None, :] * jnp.exp(
        -decay_rate[:, None, :] * (positions + 1.0)[None, :, None]
    )
    outside = jnp.einsum("jmc,mtc->jtc", starts, out_weight, precision=high)
    filtered = (inside + outside).reshape(row_count, chan_count)
    gated = (queries * (filtered + skip_gain[None, :] * mixed)).astype(jnp.bfloat16)
    return lax.all_to_all(gated, "ch", split_axis=0, concat_axis=1, tiled=True)


def solution(mesh):
    in_specs = (
        P(("ctx", "ch"), None),
        P(),
        P(None, "ctx", "ch"),
        P(None, None, "ch"),
        P(None, "ch"),
        P(None, "ch"),
        P("ch"),
    )
    out_specs = P(("ctx", "ch"), None)
    return jax.shard_map(
        on_device_body, mesh=mesh, in_specs=in_specs, out_specs=out_specs, check_vma=False
    )
```

```python
import jax
import jax.numpy as jnp
from jax import lax
from jax.sharding import PartitionSpec as P

norm_eps = 1e-05


def shifted(shard, axis, by):
    length = lax.axis_size(axis)
    pairs = [(i, i + by) for i in range(length) if 0 <= i + by < length]
    return lax.ppermute(shard, axis, pairs)


def gathered_weight(block):
    count = lax.axis_size("ctx")
    me = lax.axis_index("ctx")
    width = block.shape[1]
    held = [(block, me)]
    for by in range(2, count, 2):
        pairs = [(i, (i + by) % count) for i in range(count)]
        held.append((lax.ppermute(block, "ctx", pairs), (me - by) % count))
    sibling = [(i, i ^ 1) for i in range(count)]
    forwarded = [(lax.ppermute(part, "ctx", sibling), src ^ 1) for part, src in held]
    full = jnp.zeros((block.shape[0], count * width, block.shape[2]), block.dtype)
    for part, src in held + forwarded:
        full = lax.dynamic_update_slice(full, part, (0, src * width, 0))
    return full


def on_device_body(tokens_in, norm_gain, proj_weight, conv_weight, decay_rate, residue, skip_gain):
    widened = tokens_in.astype(jnp.float32)
    mean_square = jnp.mean(widened * widened, axis=-1, keepdims=True)
    normed = (widened * lax.rsqrt(mean_square + norm_eps) * norm_gain[None, :]).astype(jnp.bfloat16)
    feature_count = normed.shape[1]
    half = feature_count // 2
    gathered_lo = lax.all_gather(normed[:, :half], "ch", axis=0, tiled=True)
    gathered_hi = lax.all_gather(normed[:, half:], "ch", axis=0, tiled=True)
    row_count = gathered_lo.shape[0]
    chan_count = proj_weight.shape[2]
    weight = gathered_weight(proj_weight)
    summed = jnp.einsum(
        "tf,ifc->itc", gathered_lo, weight[:, :half], preferred_element_type=jnp.float32
    ) + jnp.einsum(
        "tf,ifc->itc", gathered_hi, weight[:, half:], preferred_element_type=jnp.float32
    )
    projected = summed.astype(jnp.bfloat16)
    tap_count = conv_weight.shape[1]
    reach = tap_count - 1
    rim_rows = shifted(projected[:, row_count - reach :, :], "ctx", 1)
    padded = jnp.concatenate([rim_rows, projected], axis=1).astype(jnp.float32)
    featured = jnp.zeros((3, row_count, chan_count), jnp.float32)
    for shift_idx in range(tap_count):
        featured = (
            featured
            + conv_weight[:, shift_idx, None, :]
            * padded[:, reach - shift_idx : reach - shift_idx + row_count, :]
        )
    queries = featured[0]
    mixed = featured[1] * featured[2]
    highest = lax.Precision.HIGHEST
    high = lax.Precision.HIGH
    in_scale = jnp.sqrt(-jnp.expm1(-2.0 * decay_rate))
    span_rows = min(128, row_count)
    span_count = row_count // span_rows
    positions = jnp.arange(span_rows, dtype=jnp.float32)
    own_rate, own_residue = lax.optimization_barrier((decay_rate, residue))
    own_scale = jnp.sqrt(-jnp.expm1(-2.0 * own_rate))
    lag_decay = jnp.exp(-own_rate[:, None, :] * positions[None, :, None])
    impulse = jnp.sum((own_residue * own_scale)[:, None, :] * lag_decay, axis=0)
    offsets = jnp.arange(span_rows)[:, None] - jnp.arange(span_rows)[None, :]
    lag_table = (offsets[None, :, :] == jnp.arange(span_rows)[:, None, None]).astype(jnp.float32)
    toeplitz = jnp.einsum("lc,lts->cts", impulse, lag_table, precision=highest)
    toeplitz = lax.optimization_barrier(toeplitz)
    spans_in = mixed.reshape(span_count, span_rows, chan_count)
    inside = jnp.einsum("cts,jsc->jtc", toeplitz, spans_in, precision=high)
    end_weight = in_scale[:, None, :] * jnp.exp(
        -decay_rate[:, None, :] * (span_rows - 1.0 - positions)[None, :, None]
    )
    span_ends = jnp.einsum("jsc,msc->jmc", spans_in, end_weight, precision=high)
    span_decay = jnp.exp(-decay_rate * float(span_rows))

    def advance(carried, span_end):
        return (span_decay * carried + span_end, carried)

    zero_state = jnp.zeros(decay_rate.shape, jnp.float32)
    local_end, starts = lax.scan(advance, zero_state, span_ends)
    incoming = zero_state
    for by in range(1, lax.axis_size("ctx")):
        carried_end = shifted(local_end, "ctx", by)
        incoming = incoming + jnp.exp(-decay_rate * float(row_count * (by - 1))) * carried_end
    span_starts = jnp.arange(span_count, dtype=jnp.float32) * float(span_rows)
    starts = (
        starts
        + jnp.exp(-decay_rate[None, :, :] * span_starts[:, None, None]) * incoming[None, :, :]
    )
    out_weight = residue[:, None, :] * jnp.exp(
        -decay_rate[:, None, :] * (positions + 1.0)[None, :, None]
    )
    outside = jnp.einsum("jmc,mtc->jtc", starts, out_weight, precision=high)
    filtered = (inside + outside).reshape(row_count, chan_count)
    gated = (queries * (filtered + skip_gain[None, :] * mixed)).astype(jnp.bfloat16)
    return lax.all_to_all(gated, "ch", split_axis=0, concat_axis=1, tiled=True)


def solution(mesh):
    in_specs = (
        P(("ctx", "ch"), None),
        P(),
        P(None, "ctx", "ch"),
        P(None, None, "ch"),
        P(None, "ch"),
        P(None, "ch"),
        P("ch"),
    )
    out_specs = P(("ctx", "ch"), None)
    return jax.shard_map(
        on_device_body, mesh=mesh, in_specs=in_specs, out_specs=out_specs, check_vma=False
    )
```

```python
import jax
import jax.numpy as jnp
from jax import lax
from jax.sharding import PartitionSpec as P
from jax.experimental import pallas as pl

norm_eps = 1e-05


def shifted(shard, axis, by):
    length = lax.axis_size(axis)
    pairs = [(i, i + by) for i in range(length) if 0 <= i + by < length]
    return lax.ppermute(shard, axis, pairs)


LANES = 128


def modal_kernel(x_ref, r_ref, b_ref, res_ref, y_ref, end_ref):
    half = r_ref.shape[0] // 2
    r0, r1 = r_ref[:half, :], r_ref[half:, :]
    b0, b1 = b_ref[:half, :], b_ref[half:, :]
    q0, q1 = res_ref[:half, :], res_ref[half:, :]
    rows = x_ref.shape[0]

    def step8(i, carry):
        s0, s1 = carry
        at = pl.multiple_of(i * 8, 8)
        xb = x_ref[pl.ds(at, 8), :]
        outs = []
        for k in range(8):
            xt = xb[k : k + 1, :]
            s0 = r0 * s0 + b0 * xt
            s1 = r1 * s1 + b1 * xt
            outs.append(jnp.sum(q0 * s0 + q1 * s1, axis=0, keepdims=True))
        y_ref[pl.ds(at, 8), :] = jnp.concatenate(outs, axis=0)
        return s0, s1

    zero = jnp.zeros((half, x_ref.shape[1]), jnp.float32)
    s0, s1 = lax.fori_loop(0, rows // 8, step8, (zero, zero))
    end_ref[:half, :] = s0
    end_ref[half:, :] = s1


def modal_filter(x, retention, in_scale, residue):
    rows, chans = x.shape
    modes = retention.shape[0]
    col = lambda i: (0, i)
    return pl.pallas_call(
        modal_kernel,
        grid=(chans // LANES,),
        in_specs=[
            pl.BlockSpec((rows, LANES), col),
            pl.BlockSpec((modes, LANES), col),
            pl.BlockSpec((modes, LANES), col),
            pl.BlockSpec((modes, LANES), col),
        ],
        out_specs=[pl.BlockSpec((rows, LANES), col), pl.BlockSpec((modes, LANES), col)],
        out_shape=[
            jax.ShapeDtypeStruct((rows, chans), jnp.float32),
            jax.ShapeDtypeStruct((modes, chans), jnp.float32),
        ],
    )(x, retention, in_scale, residue)


def gathered_weight(block):
    count = lax.axis_size("ctx")
    me = lax.axis_index("ctx")
    width = block.shape[1]
    held = [(block, me)]
    for by in range(2, count, 2):
        pairs = [(i, (i + by) % count) for i in range(count)]
        held.append((lax.ppermute(block, "ctx", pairs), (me - by) % count))
    sibling = [(i, i ^ 1) for i in range(count)]
    forwarded = [(lax.ppermute(part, "ctx", sibling), src ^ 1) for part, src in held]
    full = jnp.zeros((block.shape[0], count * width, block.shape[2]), block.dtype)
    for part, src in held + forwarded:
        full = lax.dynamic_update_slice(full, part, (0, src * width, 0))
    return full


def on_device_body(tokens_in, norm_gain, proj_weight, conv_weight, decay_rate, residue, skip_gain):
    widened = tokens_in.astype(jnp.float32)
    mean_square = jnp.mean(widened * widened, axis=-1, keepdims=True)
    normed = (widened * lax.rsqrt(mean_square + norm_eps) * norm_gain[None, :]).astype(jnp.bfloat16)
    gathered = lax.all_gather(normed, "ch", axis=0, tiled=True)
    row_count = gathered.shape[0]
    chan_count = proj_weight.shape[2]
    summed = jnp.einsum(
        "tf,ifc->itc",
        gathered,
        gathered_weight(proj_weight),
        preferred_element_type=jnp.float32,
    )
    projected = summed.astype(jnp.bfloat16)
    tap_count = conv_weight.shape[1]
    reach = tap_count - 1
    rim_rows = shifted(projected[:, row_count - reach :, :], "ctx", 1)
    padded = jnp.concatenate([rim_rows, projected], axis=1).astype(jnp.float32)
    featured = jnp.zeros((3, row_count, chan_count), jnp.float32)
    for shift_idx in range(tap_count):
        featured = (
            featured
            + conv_weight[:, shift_idx, None, :]
            * padded[:, reach - shift_idx : reach - shift_idx + row_count, :]
        )
    queries = featured[0]
    mixed = featured[1] * featured[2]
    high = lax.Precision.HIGH
    retention = jnp.exp(-decay_rate)
    in_scale = jnp.sqrt(-jnp.expm1(-2.0 * decay_rate))
    local_filtered, local_end = modal_filter(mixed, retention, in_scale, residue)
    zero_state = jnp.zeros(decay_rate.shape, jnp.float32)
    incoming = zero_state
    for by in range(1, lax.axis_size("ctx")):
        carried_end = shifted(local_end, "ctx", by)
        incoming = incoming + jnp.exp(-decay_rate * float(row_count * (by - 1))) * carried_end
    span_rows = min(128, row_count)
    span_count = row_count // span_rows
    positions = jnp.arange(span_rows, dtype=jnp.float32)
    span_starts = jnp.arange(span_count, dtype=jnp.float32) * float(span_rows)
    starts = jnp.exp(-decay_rate[None, :, :] * span_starts[:, None, None]) * incoming[None, :, :]
    out_weight = residue[:, None, :] * jnp.exp(
        -decay_rate[:, None, :] * (positions + 1.0)[None, :, None]
    )
    outside = jnp.einsum("jmc,mtc->jtc", starts, out_weight, precision=high)
    filtered = local_filtered + outside.reshape(row_count, chan_count)
    gated = (queries * (filtered + skip_gain[None, :] * mixed)).astype(jnp.bfloat16)
    return lax.all_to_all(gated, "ch", split_axis=0, concat_axis=1, tiled=True)


def solution(mesh):
    in_specs = (
        P(("ctx", "ch"), None),
        P(),
        P(None, "ctx", "ch"),
        P(None, None, "ch"),
        P(None, "ch"),
        P(None, "ch"),
        P("ch"),
    )
    out_specs = P(("ctx", "ch"), None)
    return jax.shard_map(
        on_device_body, mesh=mesh, in_specs=in_specs, out_specs=out_specs, check_vma=False
    )
```

```python
import jax
import jax.numpy as jnp
from jax import lax
from jax.sharding import PartitionSpec as P
from jax.experimental import pallas as pl

norm_eps = 1e-05


def shifted(shard, axis, by):
    length = lax.axis_size(axis)
    pairs = [(i, i + by) for i in range(length) if 0 <= i + by < length]
    return lax.ppermute(shard, axis, pairs)


LANES = 128


def modal_kernel(x_ref, r_ref, b_ref, res_ref, y_ref, end_ref):
    half = r_ref.shape[0] // 2
    r0, r1 = r_ref[:half, :], r_ref[half:, :]
    b0, b1 = b_ref[:half, :], b_ref[half:, :]
    q0, q1 = res_ref[:half, :], res_ref[half:, :]
    rows = x_ref.shape[0]

    def step8(i, carry):
        s0, s1 = carry
        at = pl.multiple_of(i * 8, 8)
        xb = x_ref[pl.ds(at, 8), :]
        outs = []
        for k in range(8):
            xt = xb[k : k + 1, :]
            s0 = r0 * s0 + b0 * xt
            s1 = r1 * s1 + b1 * xt
            outs.append(jnp.sum(q0 * s0 + q1 * s1, axis=0, keepdims=True))
        y_ref[pl.ds(at, 8), :] = jnp.concatenate(outs, axis=0)
        return s0, s1

    zero = jnp.zeros((half, x_ref.shape[1]), jnp.float32)
    s0, s1 = lax.fori_loop(0, rows // 8, step8, (zero, zero))
    end_ref[:half, :] = s0
    end_ref[half:, :] = s1


def modal_filter(x, retention, in_scale, residue):
    rows, chans = x.shape
    modes = retention.shape[0]
    lanes = next((w for w in (2 * LANES, LANES) if chans % w == 0), chans)
    col = lambda i: (0, i)
    return pl.pallas_call(
        modal_kernel,
        grid=(chans // lanes,),
        in_specs=[
            pl.BlockSpec((rows, lanes), col),
            pl.BlockSpec((modes, lanes), col),
            pl.BlockSpec((modes, lanes), col),
            pl.BlockSpec((modes, lanes), col),
        ],
        out_specs=[pl.BlockSpec((rows, lanes), col), pl.BlockSpec((modes, lanes), col)],
        out_shape=[
            jax.ShapeDtypeStruct((rows, chans), jnp.float32),
            jax.ShapeDtypeStruct((modes, chans), jnp.float32),
        ],
    )(x, retention, in_scale, residue)


def gathered_weight(block):
    count = lax.axis_size("ctx")
    me = lax.axis_index("ctx")
    width = block.shape[1]
    held = [(block, me)]
    for by in range(2, count, 2):
        pairs = [(i, (i + by) % count) for i in range(count)]
        held.append((lax.ppermute(block, "ctx", pairs), (me - by) % count))
    sibling = [(i, i ^ 1) for i in range(count)]
    forwarded = [(lax.ppermute(part, "ctx", sibling), src ^ 1) for part, src in held]
    full = jnp.zeros((block.shape[0], count * width, block.shape[2]), block.dtype)
    for part, src in held + forwarded:
        full = lax.dynamic_update_slice(full, part, (0, src * width, 0))
    return full


def on_device_body(tokens_in, norm_gain, proj_weight, conv_weight, decay_rate, residue, skip_gain):
    widened = tokens_in.astype(jnp.float32)
    mean_square = jnp.mean(widened * widened, axis=-1, keepdims=True)
    normed = (widened * lax.rsqrt(mean_square + norm_eps) * norm_gain[None, :]).astype(jnp.bfloat16)
    gathered = lax.all_gather(normed, "ch", axis=0, tiled=True)
    row_count = gathered.shape[0]
    chan_count = proj_weight.shape[2]
    summed = jnp.einsum(
        "tf,ifc->itc",
        gathered,
        gathered_weight(proj_weight),
        preferred_element_type=jnp.float32,
    )
    projected = summed.astype(jnp.bfloat16)
    tap_count = conv_weight.shape[1]
    reach = tap_count - 1
    rim_rows = shifted(projected[:, row_count - reach :, :], "ctx", 1)
    padded = jnp.concatenate([rim_rows, projected], axis=1).astype(jnp.float32)
    featured = jnp.zeros((3, row_count, chan_count), jnp.float32)
    for shift_idx in range(tap_count):
        featured = (
            featured
            + conv_weight[:, shift_idx, None, :]
            * padded[:, reach - shift_idx : reach - shift_idx + row_count, :]
        )
    queries = featured[0]
    mixed = featured[1] * featured[2]
    high = lax.Precision.HIGH
    retention = jnp.exp(-decay_rate)
    in_scale = jnp.sqrt(-jnp.expm1(-2.0 * decay_rate))
    local_filtered, local_end = modal_filter(mixed, retention, in_scale, residue)
    incoming = shifted(local_end, "ctx", 1)
    reach = 1
    while reach < lax.axis_size("ctx"):
        incoming = incoming + jnp.exp(-decay_rate * float(row_count * reach)) * shifted(
            incoming, "ctx", reach
        )
        reach *= 2
    span_rows = min(128, row_count)
    span_count = row_count // span_rows
    positions = jnp.arange(span_rows, dtype=jnp.float32)
    span_starts = jnp.arange(span_count, dtype=jnp.float32) * float(span_rows)
    starts = jnp.exp(-decay_rate[None, :, :] * span_starts[:, None, None]) * incoming[None, :, :]
    out_weight = residue[:, None, :] * jnp.exp(
        -decay_rate[:, None, :] * (positions + 1.0)[None, :, None]
    )
    outside = jnp.einsum("jmc,mtc->jtc", starts, out_weight, precision=high)
    filtered = local_filtered + outside.reshape(row_count, chan_count)
    gated = (queries * (filtered + skip_gain[None, :] * mixed)).astype(jnp.bfloat16)
    return lax.all_to_all(gated, "ch", split_axis=0, concat_axis=1, tiled=True)


def solution(mesh):
    in_specs = (
        P(("ctx", "ch"), None),
        P(),
        P(None, "ctx", "ch"),
        P(None, None, "ch"),
        P(None, "ch"),
        P(None, "ch"),
        P("ch"),
    )
    out_specs = P(("ctx", "ch"), None)
    return jax.shard_map(
        on_device_body, mesh=mesh, in_specs=in_specs, out_specs=out_specs, check_vma=False
    )
```

```python
import jax
import jax.numpy as jnp
from jax import lax
from jax.sharding import PartitionSpec as P
from jax.experimental import pallas as pl

norm_eps = 1e-05


def shifted(shard, axis, by):
    length = lax.axis_size(axis)
    pairs = [(i, i + by) for i in range(length) if 0 <= i + by < length]
    return lax.ppermute(shard, axis, pairs)


LANES = 128


def modal_kernel(x_ref, r_ref, b_ref, res_ref, y_ref, end_ref):
    half = r_ref.shape[0] // 2
    r0, r1 = r_ref[:half, :], r_ref[half:, :]
    b0, b1 = b_ref[:half, :], b_ref[half:, :]
    q0, q1 = res_ref[:half, :], res_ref[half:, :]
    rows = x_ref.shape[0]

    def step8(i, carry):
        s0, s1 = carry
        at = pl.multiple_of(i * 8, 8)
        xb = x_ref[pl.ds(at, 8), :]
        outs = []
        for k in range(8):
            xt = xb[k : k + 1, :]
            s0 = r0 * s0 + b0 * xt
            s1 = r1 * s1 + b1 * xt
            outs.append(jnp.sum(q0 * s0 + q1 * s1, axis=0, keepdims=True))
        y_ref[pl.ds(at, 8), :] = jnp.concatenate(outs, axis=0)
        return s0, s1

    zero = jnp.zeros((half, x_ref.shape[1]), jnp.float32)
    s0, s1 = lax.fori_loop(0, rows // 8, step8, (zero, zero))
    end_ref[:half, :] = s0
    end_ref[half:, :] = s1


def modal_filter(x, retention, in_scale, residue):
    rows, chans = x.shape
    modes = retention.shape[0]
    lanes = next((w for w in (2 * LANES, LANES) if chans % w == 0), chans)
    col = lambda i: (0, i)
    return pl.pallas_call(
        modal_kernel,
        grid=(chans // lanes,),
        in_specs=[
            pl.BlockSpec((rows, lanes), col),
            pl.BlockSpec((modes, lanes), col),
            pl.BlockSpec((modes, lanes), col),
            pl.BlockSpec((modes, lanes), col),
        ],
        out_specs=[pl.BlockSpec((rows, lanes), col), pl.BlockSpec((modes, lanes), col)],
        out_shape=[
            jax.ShapeDtypeStruct((rows, chans), jnp.float32),
            jax.ShapeDtypeStruct((modes, chans), jnp.float32),
        ],
    )(x, retention, in_scale, residue)


def gathered_weight(block):
    count = lax.axis_size("ctx")
    me = lax.axis_index("ctx")
    width = block.shape[1]
    held = [(block, me)]
    for by in range(2, count, 2):
        pairs = [(i, (i + by) % count) for i in range(count)]
        held.append((lax.ppermute(block, "ctx", pairs), (me - by) % count))
    sibling = [(i, i ^ 1) for i in range(count)]
    forwarded = [(lax.ppermute(part, "ctx", sibling), src ^ 1) for part, src in held]
    full = jnp.zeros((block.shape[0], count * width, block.shape[2]), block.dtype)
    for part, src in held + forwarded:
        full = lax.dynamic_update_slice(full, part, (0, src * width, 0))
    return full


def on_device_body(tokens_in, norm_gain, proj_weight, conv_weight, decay_rate, residue, skip_gain):
    widened = tokens_in.astype(jnp.float32)
    mean_square = jnp.mean(widened * widened, axis=-1, keepdims=True)
    normed = (widened * lax.rsqrt(mean_square + norm_eps) * norm_gain[None, :]).astype(jnp.bfloat16)
    gathered = lax.all_gather(normed, "ch", axis=0, tiled=True)
    row_count = gathered.shape[0]
    chan_count = proj_weight.shape[2]
    summed = jnp.einsum(
        "tf,ifc->itc",
        gathered,
        gathered_weight(proj_weight),
        preferred_element_type=jnp.float32,
    )
    projected = summed.astype(jnp.bfloat16)
    tap_count = conv_weight.shape[1]
    reach = tap_count - 1
    rim_rows = shifted(projected[:, row_count - reach :, :], "ctx", 1)
    padded = jnp.concatenate([rim_rows, projected], axis=1).astype(jnp.float32)
    featured = jnp.zeros((3, row_count, chan_count), jnp.float32)
    for shift_idx in range(tap_count):
        featured = (
            featured
            + conv_weight[:, shift_idx, None, :]
            * padded[:, reach - shift_idx : reach - shift_idx + row_count, :]
        )
    queries = featured[0]
    mixed = featured[1] * featured[2]
    high = lax.Precision.HIGH
    retention = jnp.exp(-decay_rate)
    in_scale = jnp.sqrt(-jnp.expm1(-2.0 * decay_rate))
    local_filtered, local_end = modal_filter(mixed, retention, in_scale, residue)
    range_count = lax.axis_size("ctx")
    later = jnp.arange(range_count) - lax.axis_index("ctx") - 1
    lag = (float(row_count) * jnp.maximum(later, 0).astype(jnp.float32))[:, None, None]
    sent = jnp.where((later >= 0)[:, None, None], jnp.exp(-decay_rate[None] * lag), 0.0)
    sent = sent * local_end[None]
    received = lax.all_to_all(sent, "ctx", split_axis=0, concat_axis=0, tiled=True)
    incoming = jnp.sum(received, axis=0)
    span_rows = min(128, row_count)
    span_count = row_count // span_rows
    positions = jnp.arange(span_rows, dtype=jnp.float32)
    span_starts = jnp.arange(span_count, dtype=jnp.float32) * float(span_rows)
    starts = jnp.exp(-decay_rate[None, :, :] * span_starts[:, None, None]) * incoming[None, :, :]
    out_weight = residue[:, None, :] * jnp.exp(
        -decay_rate[:, None, :] * (positions + 1.0)[None, :, None]
    )
    outside = jnp.einsum("jmc,mtc->jtc", starts, out_weight, precision=high)
    filtered = local_filtered + outside.reshape(row_count, chan_count)
    gated = (queries * (filtered + skip_gain[None, :] * mixed)).astype(jnp.bfloat16)
    return lax.all_to_all(gated, "ch", split_axis=0, concat_axis=1, tiled=True)


def solution(mesh):
    in_specs = (
        P(("ctx", "ch"), None),
        P(),
        P(None, "ctx", "ch"),
        P(None, None, "ch"),
        P(None, "ch"),
        P(None, "ch"),
        P("ch"),
    )
    out_specs = P(("ctx", "ch"), None)
    return jax.shard_map(
        on_device_body, mesh=mesh, in_specs=in_specs, out_specs=out_specs, check_vma=False
    )
```

```python
import jax
import jax.numpy as jnp
from jax import lax
from jax.sharding import PartitionSpec as P
from jax.experimental import pallas as pl

norm_eps = 1e-05


def shifted(shard, axis, by):
    length = lax.axis_size(axis)
    pairs = [(i, i + by) for i in range(length) if 0 <= i + by < length]
    return lax.ppermute(shard, axis, pairs)


LANES = 128


def ends_kernel(x_ref, r_ref, b_ref, end_ref):
    half = r_ref.shape[0] // 2
    r0, r1 = r_ref[:half, :], r_ref[half:, :]
    b0, b1 = b_ref[:half, :], b_ref[half:, :]

    def step8(i, carry):
        s0, s1 = carry
        xb = x_ref[pl.ds(pl.multiple_of(i * 8, 8), 8), :]
        for k in range(8):
            xt = xb[k : k + 1, :]
            s0 = r0 * s0 + b0 * xt
            s1 = r1 * s1 + b1 * xt
        return s0, s1

    zero = jnp.zeros((half, x_ref.shape[1]), jnp.float32)
    s0, s1 = lax.fori_loop(0, x_ref.shape[0] // 8, step8, (zero, zero))
    end_ref[:half, :] = s0
    end_ref[half:, :] = s1


def gate_kernel(x_ref, q_ref, r_ref, b_ref, res_ref, skip_ref, init_ref, out_ref):
    half = r_ref.shape[0] // 2
    r0, r1 = r_ref[:half, :], r_ref[half:, :]
    b0, b1 = b_ref[:half, :], b_ref[half:, :]
    q0, q1 = res_ref[:half, :], res_ref[half:, :]
    skip = skip_ref[...]

    def step16(i, carry):
        s0, s1 = carry
        at = pl.multiple_of(i * 16, 16)
        xb = x_ref[pl.ds(at, 16), :]
        outs = []
        for k in range(16):
            xt = xb[k : k + 1, :]
            s0 = r0 * s0 + b0 * xt
            s1 = r1 * s1 + b1 * xt
            outs.append(jnp.sum(q0 * s0 + q1 * s1, axis=0, keepdims=True))
        filtered = jnp.concatenate(outs, axis=0)
        out_ref[pl.ds(at, 16), :] = (q_ref[pl.ds(at, 16), :] * (filtered + skip * xb)).astype(
            out_ref.dtype
        )
        return s0, s1

    lax.fori_loop(0, x_ref.shape[0] // 16, step16, (init_ref[:half, :], init_ref[half:, :]))


def lane_block(chans):
    return next((w for w in (2 * LANES, LANES) if chans % w == 0), chans)


def modal_ends(x, retention, in_scale):
    rows, chans = x.shape
    modes = retention.shape[0]
    lanes = lane_block(chans)
    col = lambda i: (0, i)
    return pl.pallas_call(
        ends_kernel,
        grid=(chans // lanes,),
        in_specs=[
            pl.BlockSpec((rows, lanes), col),
            pl.BlockSpec((modes, lanes), col),
            pl.BlockSpec((modes, lanes), col),
        ],
        out_specs=pl.BlockSpec((modes, lanes), col),
        out_shape=jax.ShapeDtypeStruct((modes, chans), jnp.float32),
    )(x, retention, in_scale)


def modal_gate(x, queries, retention, in_scale, residue, skip_gain, incoming):
    rows, chans = x.shape
    modes = retention.shape[0]
    lanes = lane_block(chans)
    col = lambda i: (0, i)
    return pl.pallas_call(
        gate_kernel,
        grid=(chans // lanes,),
        in_specs=[
            pl.BlockSpec((rows, lanes), col),
            pl.BlockSpec((rows, lanes), col),
            pl.BlockSpec((modes, lanes), col),
            pl.BlockSpec((modes, lanes), col),
            pl.BlockSpec((modes, lanes), col),
            pl.BlockSpec((1, lanes), col),
            pl.BlockSpec((modes, lanes), col),
        ],
        out_specs=pl.BlockSpec((rows, lanes), col),
        out_shape=jax.ShapeDtypeStruct((rows, chans), jnp.bfloat16),
    )(x, queries, retention, in_scale, residue, skip_gain.reshape(1, chans), incoming)


def gathered_weight(block):
    count = lax.axis_size("ctx")
    me = lax.axis_index("ctx")
    width = block.shape[1]
    held = [(block, me)]
    for by in range(2, count, 2):
        pairs = [(i, (i + by) % count) for i in range(count)]
        held.append((lax.ppermute(block, "ctx", pairs), (me - by) % count))
    sibling = [(i, i ^ 1) for i in range(count)]
    forwarded = [(lax.ppermute(part, "ctx", sibling), src ^ 1) for part, src in held]
    full = jnp.zeros((block.shape[0], count * width, block.shape[2]), block.dtype)
    for part, src in held + forwarded:
        full = lax.dynamic_update_slice(full, part, (0, src * width, 0))
    return full


def on_device_body(tokens_in, norm_gain, proj_weight, conv_weight, decay_rate, residue, skip_gain):
    widened = tokens_in.astype(jnp.float32)
    mean_square = jnp.mean(widened * widened, axis=-1, keepdims=True)
    normed = (widened * lax.rsqrt(mean_square + norm_eps) * norm_gain[None, :]).astype(jnp.bfloat16)
    gathered = lax.all_gather(normed, "ch", axis=0, tiled=True)
    row_count = gathered.shape[0]
    chan_count = proj_weight.shape[2]
    summed = jnp.einsum(
        "tf,ifc->itc",
        gathered,
        gathered_weight(proj_weight),
        preferred_element_type=jnp.float32,
    )
    projected = summed.astype(jnp.bfloat16)
    tap_count = conv_weight.shape[1]
    reach = tap_count - 1
    rim_rows = shifted(projected[:, row_count - reach :, :], "ctx", 1)
    padded = jnp.concatenate([rim_rows, projected], axis=1).astype(jnp.float32)
    featured = jnp.zeros((3, row_count, chan_count), jnp.float32)
    for shift_idx in range(tap_count):
        featured = (
            featured
            + conv_weight[:, shift_idx, None, :]
            * padded[:, reach - shift_idx : reach - shift_idx + row_count, :]
        )
    queries = featured[0]
    mixed = featured[1] * featured[2]
    retention = jnp.exp(-decay_rate)
    in_scale = jnp.sqrt(-jnp.expm1(-2.0 * decay_rate))
    local_end = modal_ends(mixed, retention, in_scale)
    range_count = lax.axis_size("ctx")
    later = jnp.arange(range_count) - lax.axis_index("ctx") - 1
    lag = (float(row_count) * jnp.maximum(later, 0).astype(jnp.float32))[:, None, None]
    sent = jnp.where((later >= 0)[:, None, None], jnp.exp(-decay_rate[None] * lag), 0.0)
    sent = sent * local_end[None]
    received = lax.all_to_all(sent, "ctx", split_axis=0, concat_axis=0, tiled=True)
    incoming = jnp.sum(received, axis=0)
    gated = modal_gate(mixed, queries, retention, in_scale, residue, skip_gain, incoming)
    return lax.all_to_all(gated, "ch", split_axis=0, concat_axis=1, tiled=True)


def solution(mesh):
    in_specs = (
        P(("ctx", "ch"), None),
        P(),
        P(None, "ctx", "ch"),
        P(None, None, "ch"),
        P(None, "ch"),
        P(None, "ch"),
        P("ch"),
    )
    out_specs = P(("ctx", "ch"), None)
    return jax.shard_map(
        on_device_body, mesh=mesh, in_specs=in_specs, out_specs=out_specs, check_vma=False
    )
```

```python
import jax
import jax.numpy as jnp
from jax import lax
from jax.sharding import PartitionSpec as P
from jax.experimental import pallas as pl

norm_eps = 1e-05


def shifted(shard, axis, by):
    length = lax.axis_size(axis)
    pairs = [(i, i + by) for i in range(length) if 0 <= i + by < length]
    return lax.ppermute(shard, axis, pairs)


LANES = 128


CHUNKS = 4


def ends_kernel(x_ref, r_ref, b_ref, end_ref):
    half = r_ref.shape[0] // 2
    r0, r1 = r_ref[:half, :], r_ref[half:, :]
    b0, b1 = b_ref[:half, :], b_ref[half:, :]
    chunks = end_ref.shape[0]
    span = x_ref.shape[0] // chunks

    def step8(i, carry):
        carry = list(carry)
        at = pl.multiple_of(i * 8, 8)
        for c in range(chunks):
            s0, s1 = carry[2 * c], carry[2 * c + 1]
            xb = x_ref[pl.ds(c * span + at, 8), :]
            for k in range(8):
                xt = xb[k : k + 1, :]
                s0 = r0 * s0 + b0 * xt
                s1 = r1 * s1 + b1 * xt
            carry[2 * c], carry[2 * c + 1] = s0, s1
        return tuple(carry)

    zero = jnp.zeros((half, x_ref.shape[1]), jnp.float32)
    ends = lax.fori_loop(0, span // 8, step8, (zero,) * (2 * chunks))
    for c in range(chunks):
        end_ref[c, :half, :] = ends[2 * c]
        end_ref[c, half:, :] = ends[2 * c + 1]


def gate_kernel(x_ref, q_ref, r_ref, b_ref, res_ref, skip_ref, init_ref, out_ref):
    half = r_ref.shape[0] // 2
    r0, r1 = r_ref[:half, :], r_ref[half:, :]
    b0, b1 = b_ref[:half, :], b_ref[half:, :]
    q0, q1 = res_ref[:half, :], res_ref[half:, :]
    skip = skip_ref[...]
    chunks = init_ref.shape[0]
    span = x_ref.shape[0] // chunks

    def step16(i, carry):
        carry = list(carry)
        at = pl.multiple_of(i * 16, 16)
        for c in range(chunks):
            s0, s1 = carry[2 * c], carry[2 * c + 1]
            rows = pl.ds(c * span + at, 16)
            xb = x_ref[rows, :]
            outs = []
            for k in range(16):
                xt = xb[k : k + 1, :]
                s0 = r0 * s0 + b0 * xt
                s1 = r1 * s1 + b1 * xt
                outs.append(jnp.sum(q0 * s0 + q1 * s1, axis=0, keepdims=True))
            filtered = jnp.concatenate(outs, axis=0)
            out_ref[rows, :] = (q_ref[rows, :] * (filtered + skip * xb)).astype(out_ref.dtype)
            carry[2 * c], carry[2 * c + 1] = s0, s1
        return tuple(carry)

    init = []
    for c in range(chunks):
        init += [init_ref[c, :half, :], init_ref[c, half:, :]]
    lax.fori_loop(0, span // 16, step16, tuple(init))


def lane_block(chans):
    return next((w for w in (2 * LANES, LANES) if chans % w == 0), chans)


def modal_ends(x, retention, in_scale):
    rows, chans = x.shape
    modes = retention.shape[0]
    lanes = lane_block(chans)
    col = lambda i: (0, i)
    return pl.pallas_call(
        ends_kernel,
        grid=(chans // lanes,),
        in_specs=[
            pl.BlockSpec((rows, lanes), col),
            pl.BlockSpec((modes, lanes), col),
            pl.BlockSpec((modes, lanes), col),
        ],
        out_specs=pl.BlockSpec((CHUNKS, modes, lanes), lambda i: (0, 0, i)),
        out_shape=jax.ShapeDtypeStruct((CHUNKS, modes, chans), jnp.float32),
    )(x, retention, in_scale)


def modal_gate(x, queries, retention, in_scale, residue, skip_gain, incoming):
    rows, chans = x.shape
    modes = retention.shape[0]
    lanes = lane_block(chans)
    col = lambda i: (0, i)
    return pl.pallas_call(
        gate_kernel,
        grid=(chans // lanes,),
        in_specs=[
            pl.BlockSpec((rows, lanes), col),
            pl.BlockSpec((rows, lanes), col),
            pl.BlockSpec((modes, lanes), col),
            pl.BlockSpec((modes, lanes), col),
            pl.BlockSpec((modes, lanes), col),
            pl.BlockSpec((1, lanes), col),
            pl.BlockSpec((CHUNKS, modes, lanes), lambda i: (0, 0, i)),
        ],
        out_specs=pl.BlockSpec((rows, lanes), col),
        out_shape=jax.ShapeDtypeStruct((rows, chans), jnp.bfloat16),
    )(x, queries, retention, in_scale, residue, skip_gain.reshape(1, chans), incoming)


def gathered_weight(block):
    count = lax.axis_size("ctx")
    me = lax.axis_index("ctx")
    width = block.shape[1]
    held = [(block, me)]
    for by in range(2, count, 2):
        pairs = [(i, (i + by) % count) for i in range(count)]
        held.append((lax.ppermute(block, "ctx", pairs), (me - by) % count))
    sibling = [(i, i ^ 1) for i in range(count)]
    forwarded = [(lax.ppermute(part, "ctx", sibling), src ^ 1) for part, src in held]
    full = jnp.zeros((block.shape[0], count * width, block.shape[2]), block.dtype)
    for part, src in held + forwarded:
        full = lax.dynamic_update_slice(full, part, (0, src * width, 0))
    return full


def on_device_body(tokens_in, norm_gain, proj_weight, conv_weight, decay_rate, residue, skip_gain):
    widened = tokens_in.astype(jnp.float32)
    mean_square = jnp.mean(widened * widened, axis=-1, keepdims=True)
    normed = (widened * lax.rsqrt(mean_square + norm_eps) * norm_gain[None, :]).astype(jnp.bfloat16)
    gathered = lax.all_gather(normed, "ch", axis=0, tiled=True)
    row_count = gathered.shape[0]
    chan_count = proj_weight.shape[2]
    summed = jnp.einsum(
        "tf,ifc->itc",
        gathered,
        gathered_weight(proj_weight),
        preferred_element_type=jnp.float32,
    )
    projected = summed.astype(jnp.bfloat16)
    tap_count = conv_weight.shape[1]
    reach = tap_count - 1
    rim_rows = shifted(projected[:, row_count - reach :, :], "ctx", 1)
    padded = jnp.concatenate([rim_rows, projected], axis=1).astype(jnp.float32)
    featured = jnp.zeros((3, row_count, chan_count), jnp.float32)
    for shift_idx in range(tap_count):
        featured = (
            featured
            + conv_weight[:, shift_idx, None, :]
            * padded[:, reach - shift_idx : reach - shift_idx + row_count, :]
        )
    queries = featured[0]
    mixed = featured[1] * featured[2]
    retention = jnp.exp(-decay_rate)
    in_scale = jnp.sqrt(-jnp.expm1(-2.0 * decay_rate))
    chunk_ends = modal_ends(mixed, retention, in_scale)
    chunk_decay = jnp.exp(-decay_rate * float(row_count // CHUNKS))
    local_end = chunk_ends[0]
    for c in range(1, CHUNKS):
        local_end = chunk_decay * local_end + chunk_ends[c]
    range_count = lax.axis_size("ctx")
    later = jnp.arange(range_count) - lax.axis_index("ctx") - 1
    lag = (float(row_count) * jnp.maximum(later, 0).astype(jnp.float32))[:, None, None]
    sent = jnp.where((later >= 0)[:, None, None], jnp.exp(-decay_rate[None] * lag), 0.0)
    sent = sent * local_end[None]
    received = lax.all_to_all(sent, "ctx", split_axis=0, concat_axis=0, tiled=True)
    starts = [jnp.sum(received, axis=0)]
    for c in range(1, CHUNKS):
        starts.append(chunk_decay * starts[-1] + chunk_ends[c - 1])
    incoming = jnp.stack(starts)
    gated = modal_gate(mixed, queries, retention, in_scale, residue, skip_gain, incoming)
    return lax.all_to_all(gated, "ch", split_axis=0, concat_axis=1, tiled=True)


def solution(mesh):
    in_specs = (
        P(("ctx", "ch"), None),
        P(),
        P(None, "ctx", "ch"),
        P(None, None, "ch"),
        P(None, "ch"),
        P(None, "ch"),
        P("ch"),
    )
    out_specs = P(("ctx", "ch"), None)
    return jax.shard_map(
        on_device_body, mesh=mesh, in_specs=in_specs, out_specs=out_specs, check_vma=False
    )
```

```python
import jax
import jax.numpy as jnp
from jax import lax
from jax.sharding import PartitionSpec as P
from jax.experimental import pallas as pl

norm_eps = 1e-05


def shifted(shard, axis, by):
    length = lax.axis_size(axis)
    pairs = [(i, i + by) for i in range(length) if 0 <= i + by < length]
    return lax.ppermute(shard, axis, pairs)


LANES = 128


def ends_kernel(x_ref, r_ref, b_ref, end_ref):
    half = r_ref.shape[0] // 2
    r0, r1 = r_ref[:half, :], r_ref[half:, :]
    b0, b1 = b_ref[:half, :], b_ref[half:, :]

    def step8(i, carry):
        s0, s1 = carry
        xb = x_ref[pl.ds(pl.multiple_of(i * 8, 8), 8), :]
        for k in range(8):
            xt = xb[k : k + 1, :]
            s0 = r0 * s0 + b0 * xt
            s1 = r1 * s1 + b1 * xt
        return s0, s1

    zero = jnp.zeros((half, x_ref.shape[1]), jnp.float32)
    s0, s1 = lax.fori_loop(0, x_ref.shape[0] // 8, step8, (zero, zero))
    end_ref[:half, :] = s0
    end_ref[half:, :] = s1


def gate_kernel(x_ref, q_ref, r_ref, b_ref, res_ref, skip_ref, init_ref, out_ref):
    half = r_ref.shape[0] // 2
    r0, r1 = r_ref[:half, :], r_ref[half:, :]
    b0, b1 = b_ref[:half, :], b_ref[half:, :]
    q0, q1 = res_ref[:half, :], res_ref[half:, :]
    skip = skip_ref[...]

    def step16(i, carry):
        s0, s1 = carry
        at = pl.multiple_of(i * 16, 16)
        xb = x_ref[pl.ds(at, 16), :]
        outs = []
        for k in range(16):
            xt = xb[k : k + 1, :]
            s0 = r0 * s0 + b0 * xt
            s1 = r1 * s1 + b1 * xt
            outs.append(jnp.sum(q0 * s0 + q1 * s1, axis=0, keepdims=True))
        filtered = jnp.concatenate(outs, axis=0)
        out_ref[pl.ds(at, 16), :] = (q_ref[pl.ds(at, 16), :] * (filtered + skip * xb)).astype(
            out_ref.dtype
        )
        return s0, s1

    lax.fori_loop(0, x_ref.shape[0] // 16, step16, (init_ref[:half, :], init_ref[half:, :]))


def lane_block(chans):
    return next((w for w in (2 * LANES, LANES) if chans % w == 0), chans)


def modal_ends(x, retention, in_scale):
    rows, chans = x.shape
    modes = retention.shape[0]
    lanes = lane_block(chans)
    col = lambda i: (0, i)
    return pl.pallas_call(
        ends_kernel,
        grid=(chans // lanes,),
        in_specs=[
            pl.BlockSpec((rows, lanes), col),
            pl.BlockSpec((modes, lanes), col),
            pl.BlockSpec((modes, lanes), col),
        ],
        out_specs=pl.BlockSpec((modes, lanes), col),
        out_shape=jax.ShapeDtypeStruct((modes, chans), jnp.float32),
    )(x, retention, in_scale)


def modal_gate(x, queries, retention, in_scale, residue, skip_gain, incoming):
    rows, chans = x.shape
    modes = retention.shape[0]
    lanes = lane_block(chans)
    col = lambda i: (0, i)
    return pl.pallas_call(
        gate_kernel,
        grid=(chans // lanes,),
        in_specs=[
            pl.BlockSpec((rows, lanes), col),
            pl.BlockSpec((rows, lanes), col),
            pl.BlockSpec((modes, lanes), col),
            pl.BlockSpec((modes, lanes), col),
            pl.BlockSpec((modes, lanes), col),
            pl.BlockSpec((1, lanes), col),
            pl.BlockSpec((modes, lanes), col),
        ],
        out_specs=pl.BlockSpec((rows, lanes), col),
        out_shape=jax.ShapeDtypeStruct((rows, chans), jnp.bfloat16),
    )(x, queries, retention, in_scale, residue, skip_gain.reshape(1, chans), incoming)


def gathered_weight(block):
    count = lax.axis_size("ctx")
    me = lax.axis_index("ctx")
    width = block.shape[1]
    held = [(block, me)]
    for by in range(2, count, 2):
        pairs = [(i, (i + by) % count) for i in range(count)]
        held.append((lax.ppermute(block, "ctx", pairs), (me - by) % count))
    sibling = [(i, i ^ 1) for i in range(count)]
    forwarded = [(lax.ppermute(part, "ctx", sibling), src ^ 1) for part, src in held]
    full = jnp.zeros((block.shape[0], count * width, block.shape[2]), block.dtype)
    for part, src in held + forwarded:
        full = lax.dynamic_update_slice(full, part, (0, src * width, 0))
    return full


def on_device_body(tokens_in, norm_gain, proj_weight, conv_weight, decay_rate, residue, skip_gain):
    widened = tokens_in.astype(jnp.float32)
    mean_square = jnp.mean(widened * widened, axis=-1, keepdims=True)
    normed = (widened * lax.rsqrt(mean_square + norm_eps) * norm_gain[None, :]).astype(jnp.bfloat16)
    gathered = lax.all_gather(normed, "ch", axis=0, tiled=True)
    row_count = gathered.shape[0]
    weight = gathered_weight(proj_weight)

    def featured_of(part):
        summed = jnp.einsum(
            "tf,ifc->itc", gathered, weight[part], preferred_element_type=jnp.float32
        )
        projected = summed.astype(jnp.bfloat16)
        tap_count = conv_weight.shape[1]
        reach = tap_count - 1
        rim_rows = shifted(projected[:, row_count - reach :, :], "ctx", 1)
        padded = jnp.concatenate([rim_rows, projected], axis=1).astype(jnp.float32)
        taps = conv_weight[part]
        featured = jnp.zeros(projected.shape, jnp.float32)
        for shift_idx in range(tap_count):
            featured = (
                featured
                + taps[:, shift_idx, None, :]
                * padded[:, reach - shift_idx : reach - shift_idx + row_count, :]
            )
        return featured

    keys_values = featured_of(slice(1, 3))
    mixed = keys_values[0] * keys_values[1]
    retention = jnp.exp(-decay_rate)
    in_scale = jnp.sqrt(-jnp.expm1(-2.0 * decay_rate))
    local_end = modal_ends(mixed, retention, in_scale)
    range_count = lax.axis_size("ctx")
    later = jnp.arange(range_count) - lax.axis_index("ctx") - 1
    lag = (float(row_count) * jnp.maximum(later, 0).astype(jnp.float32))[:, None, None]
    sent = jnp.where((later >= 0)[:, None, None], jnp.exp(-decay_rate[None] * lag), 0.0)
    sent = sent * local_end[None]
    received = lax.all_to_all(sent, "ctx", split_axis=0, concat_axis=0, tiled=True)
    incoming = jnp.sum(received, axis=0)
    queries = featured_of(slice(0, 1))[0]
    gated = modal_gate(mixed, queries, retention, in_scale, residue, skip_gain, incoming)
    return lax.all_to_all(gated, "ch", split_axis=0, concat_axis=1, tiled=True)


def solution(mesh):
    in_specs = (
        P(("ctx", "ch"), None),
        P(),
        P(None, "ctx", "ch"),
        P(None, None, "ch"),
        P(None, "ch"),
        P(None, "ch"),
        P("ch"),
    )
    out_specs = P(("ctx", "ch"), None)
    return jax.shard_map(
        on_device_body, mesh=mesh, in_specs=in_specs, out_specs=out_specs, check_vma=False
    )
```

```python
import jax
import jax.numpy as jnp
from jax import lax
from jax.sharding import PartitionSpec as P
from jax.experimental import pallas as pl

norm_eps = 1e-05


def shifted(shard, axis, by):
    length = lax.axis_size(axis)
    pairs = [(i, i + by) for i in range(length) if 0 <= i + by < length]
    return lax.ppermute(shard, axis, pairs)


LANES = 128


def ends_kernel(x_ref, r_ref, b_ref, end_ref):
    half = r_ref.shape[0] // 2
    r0, r1 = r_ref[:half, :], r_ref[half:, :]
    b0, b1 = b_ref[:half, :], b_ref[half:, :]

    def step8(i, carry):
        s0, s1 = carry
        xb = x_ref[pl.ds(pl.multiple_of(i * 8, 8), 8), :]
        for k in range(8):
            xt = xb[k : k + 1, :]
            s0 = r0 * s0 + b0 * xt
            s1 = r1 * s1 + b1 * xt
        return s0, s1

    zero = jnp.zeros((half, x_ref.shape[1]), jnp.float32)
    s0, s1 = lax.fori_loop(0, x_ref.shape[0] // 8, step8, (zero, zero))
    end_ref[:half, :] = s0
    end_ref[half:, :] = s1


def gate_kernel(x_ref, q_ref, r_ref, b_ref, res_ref, skip_ref, init_ref, out_ref):
    half = r_ref.shape[0] // 2
    r0, r1 = r_ref[:half, :], r_ref[half:, :]
    b0, b1 = b_ref[:half, :], b_ref[half:, :]
    q0, q1 = res_ref[:half, :], res_ref[half:, :]
    skip = skip_ref[...]

    def step16(i, carry):
        s0, s1 = carry
        at = pl.multiple_of(i * 16, 16)
        xb = x_ref[pl.ds(at, 16), :]
        outs = []
        for k in range(16):
            xt = xb[k : k + 1, :]
            s0 = r0 * s0 + b0 * xt
            s1 = r1 * s1 + b1 * xt
            outs.append(jnp.sum(q0 * s0 + q1 * s1, axis=0, keepdims=True))
        filtered = jnp.concatenate(outs, axis=0)
        out_ref[pl.ds(at, 16), :] = (q_ref[pl.ds(at, 16), :] * (filtered + skip * xb)).astype(
            out_ref.dtype
        )
        return s0, s1

    lax.fori_loop(0, x_ref.shape[0] // 16, step16, (init_ref[:half, :], init_ref[half:, :]))


def lane_block(chans):
    return next((w for w in (2 * LANES, LANES) if chans % w == 0), chans)


def modal_ends(x, retention, in_scale):
    rows, chans = x.shape
    modes = retention.shape[0]
    lanes = lane_block(chans)
    col = lambda i: (0, i)
    return pl.pallas_call(
        ends_kernel,
        grid=(chans // lanes,),
        in_specs=[
            pl.BlockSpec((rows, lanes), col),
            pl.BlockSpec((modes, lanes), col),
            pl.BlockSpec((modes, lanes), col),
        ],
        out_specs=pl.BlockSpec((modes, lanes), col),
        out_shape=jax.ShapeDtypeStruct((modes, chans), jnp.float32),
    )(x, retention, in_scale)


def modal_gate(x, queries, retention, in_scale, residue, skip_gain, incoming):
    rows, chans = x.shape
    modes = retention.shape[0]
    lanes = lane_block(chans)
    col = lambda i: (0, i)
    return pl.pallas_call(
        gate_kernel,
        grid=(chans // lanes,),
        in_specs=[
            pl.BlockSpec((rows, lanes), col),
            pl.BlockSpec((rows, lanes), col),
            pl.BlockSpec((modes, lanes), col),
            pl.BlockSpec((modes, lanes), col),
            pl.BlockSpec((modes, lanes), col),
            pl.BlockSpec((1, lanes), col),
            pl.BlockSpec((modes, lanes), col),
        ],
        out_specs=pl.BlockSpec((rows, lanes), col),
        out_shape=jax.ShapeDtypeStruct((rows, chans), jnp.bfloat16),
    )(x, queries, retention, in_scale, residue, skip_gain.reshape(1, chans), incoming)


def norm_kernel(x_ref, gain_ref, out_ref):
    widened = x_ref[...].astype(jnp.float32)
    mean_square = jnp.mean(widened * widened, axis=-1, keepdims=True)
    out_ref[...] = (widened * lax.rsqrt(mean_square + norm_eps) * gain_ref[...]).astype(out_ref.dtype)


def rms_norm(tokens, gain):
    rows, width = tokens.shape
    return pl.pallas_call(
        norm_kernel,
        grid=(1,),
        in_specs=[
            pl.BlockSpec((rows, width), lambda i: (0, 0)),
            pl.BlockSpec((1, width), lambda i: (0, 0)),
        ],
        out_specs=pl.BlockSpec((rows, width), lambda i: (0, 0)),
        out_shape=jax.ShapeDtypeStruct((rows, width), jnp.bfloat16),
    )(tokens, gain.reshape(1, width))


def gathered_weight(block):
    count = lax.axis_size("ctx")
    me = lax.axis_index("ctx")
    width = block.shape[1]
    held = [(block, me)]
    for by in range(2, count, 2):
        pairs = [(i, (i + by) % count) for i in range(count)]
        held.append((lax.ppermute(block, "ctx", pairs), (me - by) % count))
    sibling = [(i, i ^ 1) for i in range(count)]
    forwarded = [(lax.ppermute(part, "ctx", sibling), src ^ 1) for part, src in held]
    full = jnp.zeros((block.shape[0], count * width, block.shape[2]), block.dtype)
    for part, src in held + forwarded:
        full = lax.dynamic_update_slice(full, part, (0, src * width, 0))
    return full


def on_device_body(tokens_in, norm_gain, proj_weight, conv_weight, decay_rate, residue, skip_gain):
    normed = rms_norm(tokens_in, norm_gain)
    gathered = lax.all_gather(normed, "ch", axis=0, tiled=True)
    row_count = gathered.shape[0]
    chan_count = proj_weight.shape[2]
    summed = jnp.einsum(
        "tf,ifc->itc",
        gathered,
        gathered_weight(proj_weight),
        preferred_element_type=jnp.float32,
    )
    projected = summed.astype(jnp.bfloat16)
    tap_count = conv_weight.shape[1]
    reach = tap_count - 1
    rim_rows = shifted(projected[:, row_count - reach :, :], "ctx", 1)
    padded = jnp.concatenate([rim_rows, projected], axis=1).astype(jnp.float32)
    featured = jnp.zeros((3, row_count, chan_count), jnp.float32)
    for shift_idx in range(tap_count):
        featured = (
            featured
            + conv_weight[:, shift_idx, None, :]
            * padded[:, reach - shift_idx : reach - shift_idx + row_count, :]
        )
    queries = featured[0]
    mixed = featured[1] * featured[2]
    retention = jnp.exp(-decay_rate)
    in_scale = jnp.sqrt(-jnp.expm1(-2.0 * decay_rate))
    local_end = modal_ends(mixed, retention, in_scale)
    range_count = lax.axis_size("ctx")
    later = jnp.arange(range_count) - lax.axis_index("ctx") - 1
    lag = (float(row_count) * jnp.maximum(later, 0).astype(jnp.float32))[:, None, None]
    sent = jnp.where((later >= 0)[:, None, None], jnp.exp(-decay_rate[None] * lag), 0.0)
    sent = sent * local_end[None]
    received = lax.all_to_all(sent, "ctx", split_axis=0, concat_axis=0, tiled=True)
    incoming = jnp.sum(received, axis=0)
    gated = modal_gate(mixed, queries, retention, in_scale, residue, skip_gain, incoming)
    return lax.all_to_all(gated, "ch", split_axis=0, concat_axis=1, tiled=True)


def solution(mesh):
    in_specs = (
        P(("ctx", "ch"), None),
        P(),
        P(None, "ctx", "ch"),
        P(None, None, "ch"),
        P(None, "ch"),
        P(None, "ch"),
        P("ch"),
    )
    out_specs = P(("ctx", "ch"), None)
    return jax.shard_map(
        on_device_body, mesh=mesh, in_specs=in_specs, out_specs=out_specs, check_vma=False
    )
```

```python
import jax
import jax.numpy as jnp
from jax import lax
from jax.sharding import PartitionSpec as P
from jax.experimental import pallas as pl

norm_eps = 1e-05


def shifted(shard, axis, by):
    length = lax.axis_size(axis)
    pairs = [(i, i + by) for i in range(length) if 0 <= i + by < length]
    return lax.ppermute(shard, axis, pairs)


LANES = 128


CHUNKS = 8


def ends_kernel(x_ref, r_ref, b_ref, end_ref):
    half = r_ref.shape[0] // 2
    r0, r1 = r_ref[:half, :], r_ref[half:, :]
    b0, b1 = b_ref[:half, :], b_ref[half:, :]
    chunks = end_ref.shape[0]
    span = x_ref.shape[0] // chunks

    def step8(i, carry):
        carry = list(carry)
        at = pl.multiple_of(i * 8, 8)
        for c in range(chunks):
            s0, s1 = carry[2 * c], carry[2 * c + 1]
            xb = x_ref[pl.ds(c * span + at, 8), :]
            for k in range(8):
                xt = xb[k : k + 1, :]
                s0 = r0 * s0 + b0 * xt
                s1 = r1 * s1 + b1 * xt
            carry[2 * c], carry[2 * c + 1] = s0, s1
        return tuple(carry)

    zero = jnp.zeros((half, x_ref.shape[1]), jnp.float32)
    ends = lax.fori_loop(0, span // 8, step8, (zero,) * (2 * chunks))
    for c in range(chunks):
        end_ref[c, :half, :] = ends[2 * c]
        end_ref[c, half:, :] = ends[2 * c + 1]


def gate_kernel(x_ref, q_ref, r_ref, b_ref, res_ref, skip_ref, init_ref, out_ref):
    half = r_ref.shape[0] // 2
    r0, r1 = r_ref[:half, :], r_ref[half:, :]
    b0, b1 = b_ref[:half, :], b_ref[half:, :]
    q0, q1 = res_ref[:half, :], res_ref[half:, :]
    skip = skip_ref[...]

    def step16(i, carry):
        s0, s1 = carry
        at = pl.multiple_of(i * 16, 16)
        xb = x_ref[pl.ds(at, 16), :]
        outs = []
        for k in range(16):
            xt = xb[k : k + 1, :]
            s0 = r0 * s0 + b0 * xt
            s1 = r1 * s1 + b1 * xt
            outs.append(jnp.sum(q0 * s0 + q1 * s1, axis=0, keepdims=True))
        filtered = jnp.concatenate(outs, axis=0)
        out_ref[pl.ds(at, 16), :] = (q_ref[pl.ds(at, 16), :] * (filtered + skip * xb)).astype(
            out_ref.dtype
        )
        return s0, s1

    lax.fori_loop(0, x_ref.shape[0] // 16, step16, (init_ref[:half, :], init_ref[half:, :]))


def lane_block(chans):
    return next((w for w in (2 * LANES, LANES) if chans % w == 0), chans)


def modal_ends(x, retention, in_scale):
    rows, chans = x.shape
    modes = retention.shape[0]
    lanes = lane_block(chans)
    col = lambda i: (0, i)
    return pl.pallas_call(
        ends_kernel,
        grid=(chans // lanes,),
        in_specs=[
            pl.BlockSpec((rows, lanes), col),
            pl.BlockSpec((modes, lanes), col),
            pl.BlockSpec((modes, lanes), col),
        ],
        out_specs=pl.BlockSpec((CHUNKS, modes, lanes), lambda i: (0, 0, i)),
        out_shape=jax.ShapeDtypeStruct((CHUNKS, modes, chans), jnp.float32),
    )(x, retention, in_scale)


def modal_gate(x, queries, retention, in_scale, residue, skip_gain, incoming):
    rows, chans = x.shape
    modes = retention.shape[0]
    lanes = lane_block(chans)
    col = lambda i: (0, i)
    return pl.pallas_call(
        gate_kernel,
        grid=(chans // lanes,),
        in_specs=[
            pl.BlockSpec((rows, lanes), col),
            pl.BlockSpec((rows, lanes), col),
            pl.BlockSpec((modes, lanes), col),
            pl.BlockSpec((modes, lanes), col),
            pl.BlockSpec((modes, lanes), col),
            pl.BlockSpec((1, lanes), col),
            pl.BlockSpec((modes, lanes), col),
        ],
        out_specs=pl.BlockSpec((rows, lanes), col),
        out_shape=jax.ShapeDtypeStruct((rows, chans), jnp.bfloat16),
    )(x, queries, retention, in_scale, residue, skip_gain.reshape(1, chans), incoming)


def gathered_weight(block):
    count = lax.axis_size("ctx")
    me = lax.axis_index("ctx")
    width = block.shape[1]
    held = [(block, me)]
    for by in range(2, count, 2):
        pairs = [(i, (i + by) % count) for i in range(count)]
        held.append((lax.ppermute(block, "ctx", pairs), (me - by) % count))
    sibling = [(i, i ^ 1) for i in range(count)]
    forwarded = [(lax.ppermute(part, "ctx", sibling), src ^ 1) for part, src in held]
    full = jnp.zeros((block.shape[0], count * width, block.shape[2]), block.dtype)
    for part, src in held + forwarded:
        full = lax.dynamic_update_slice(full, part, (0, src * width, 0))
    return full


def on_device_body(tokens_in, norm_gain, proj_weight, conv_weight, decay_rate, residue, skip_gain):
    widened = tokens_in.astype(jnp.float32)
    mean_square = jnp.mean(widened * widened, axis=-1, keepdims=True)
    normed = (widened * lax.rsqrt(mean_square + norm_eps) * norm_gain[None, :]).astype(jnp.bfloat16)
    gathered = lax.all_gather(normed, "ch", axis=0, tiled=True)
    row_count = gathered.shape[0]
    chan_count = proj_weight.shape[2]
    summed = jnp.einsum(
        "tf,ifc->itc",
        gathered,
        gathered_weight(proj_weight),
        preferred_element_type=jnp.float32,
    )
    projected = summed.astype(jnp.bfloat16)
    tap_count = conv_weight.shape[1]
    reach = tap_count - 1
    rim_rows = shifted(projected[:, row_count - reach :, :], "ctx", 1)
    padded = jnp.concatenate([rim_rows, projected], axis=1).astype(jnp.float32)
    featured = jnp.zeros((3, row_count, chan_count), jnp.float32)
    for shift_idx in range(tap_count):
        featured = (
            featured
            + conv_weight[:, shift_idx, None, :]
            * padded[:, reach - shift_idx : reach - shift_idx + row_count, :]
        )
    queries = featured[0]
    mixed = featured[1] * featured[2]
    retention = jnp.exp(-decay_rate)
    in_scale = jnp.sqrt(-jnp.expm1(-2.0 * decay_rate))
    chunk_ends = modal_ends(mixed, retention, in_scale)
    chunk_decay = jnp.exp(-decay_rate * float(row_count // CHUNKS))
    local_end = chunk_ends[0]
    for c in range(1, CHUNKS):
        local_end = chunk_decay * local_end + chunk_ends[c]
    range_count = lax.axis_size("ctx")
    later = jnp.arange(range_count) - lax.axis_index("ctx") - 1
    lag = (float(row_count) * jnp.maximum(later, 0).astype(jnp.float32))[:, None, None]
    sent = jnp.where((later >= 0)[:, None, None], jnp.exp(-decay_rate[None] * lag), 0.0)
    sent = sent * local_end[None]
    received = lax.all_to_all(sent, "ctx", split_axis=0, concat_axis=0, tiled=True)
    incoming = jnp.sum(received, axis=0)
    gated = modal_gate(mixed, queries, retention, in_scale, residue, skip_gain, incoming)
    return lax.all_to_all(gated, "ch", split_axis=0, concat_axis=1, tiled=True)


def solution(mesh):
    in_specs = (
        P(("ctx", "ch"), None),
        P(),
        P(None, "ctx", "ch"),
        P(None, None, "ch"),
        P(None, "ch"),
        P(None, "ch"),
        P("ch"),
    )
    out_specs = P(("ctx", "ch"), None)
    return jax.shard_map(
        on_device_body, mesh=mesh, in_specs=in_specs, out_specs=out_specs, check_vma=False
    )
```
